256 devices in a mesh: pipe: 16 (over y, z_hi), expert: 16 (over z_lo, x, core).
Axes of the slice: x: 4, y: 4, z: 8 (z_hi: 4, z_lo: 2; z = z_hi * 2 + z_lo), core: 2. Of those that a mesh axis runs over, the one named last changes fastest.
Arguments:
- up_in: bfloat16 [16, 1024, 2560], P('pipe', 'expert'), may hold values from -6 to 6
- down_in: bfloat16 [16, 1024, 2560], P('pipe', 'expert'), may hold values from -6 to 6
- up_ids: int32 [16, 1024, 6], P('pipe', 'expert'), may hold values from 0 to 15, all different within a row; in each aligned block of 64 rows (0 to 63, 64 to 127, ..., all dimensions but the last counted through in order) at most 32 rows name the same one
- down_ids: int32 [16, 1024, 6], P('pipe', 'expert'), may hold values from 0 to 15, all different within a row; in each aligned block of 64 rows (0 to 63, 64 to 127, ..., all dimensions but the last counted through in order) at most 32 rows name the same one
- norm_gain: float32 [16, 2560], P('pipe'), may hold values from 0.1 to 1.9
- router: bfloat16 [16, 2560, 16], P('pipe'), may hold values from -0.25 to 0.25
- w_up: bfloat16 [16, 16, 2560, 1152], P('pipe', 'expert'), may hold values from -0.125 to 0.125
- w_down: bfloat16 [16, 16, 1152, 2560], P('pipe', 'expert'), may hold values from -0.375 to 0.375
Outputs:
- up_out: bfloat16 [16, 1024, 2560], P('pipe', 'expert')
- down_out: bfloat16 [16, 1024, 2560], P('pipe', 'expert')
The draws below stay inside these ranges and needn't reach their ends.
Inputs may be any that keep to these rules, and one draw needn't show every extreme that they name: `up_ids`: each token names 6 different experts. Within the tokens of one device (aligned blocks of 64 tokens of one section) no expert is named more than 32 times, and in every draw some expert is named exactly 32 times in some block. `down_ids`: as for up_ids.
All inputs are finite; a program needn't handle non-finite values.
Results may differ from the reference program's by a relative error of at most 0.0061.
Values may be sent and summed in bfloat16 or wider, within the bound.
No kernel may reach another device: no remote copies, remote signals or barrier semaphores. Data moves between devices by JAX's collectives and lax.ppermute only.
A program may use at most 128 MiB of HBM per device.

```python
import math
import jax
import jax.numpy as jnp
import numpy as np
from jax import lax

D = 2560
FFW = 1152
EXPERTS = 16
TOP = 6
TOK_DEV = 64
CAP = 32
SECTIONS = 16
TOKENS = 1024
N_EXPERT = 16


def block_levels(key, extent, cuts, least, largest):
    level, own = 1.0, jax.random.fold_in(key, 6)
    for dim, blocks in cuts:
        draws = jnp.exp(jax.random.uniform(jax.random.fold_in(own, dim), (blocks,), jnp.float32, least / len(cuts), largest / len(cuts)))
        level = level * jnp.repeat(draws, extent[dim] // blocks).reshape([-1 if axis == dim else 1 for axis in range(len(extent))])
    return level


def assign_block(rng, own, number, rows, number_of, top, limit, lean):
    order = jax.random.permutation(rng, number_of)
    heavy_load, common = load_shares(number_of, rows * top, limit, lean, True), load_shares(number_of, rows * top, limit, lean, False)
    places = jnp.arange(number_of)

    def named(lengths, rotation):
        used = int((lengths > 0).sum())
        fixed = max(1, used // 4)
        shifted = fixed + (places - fixed + rotation * (used - fixed)) % max(1, number_of - fixed)
        return jnp.zeros((number_of,), jnp.int32).at[order[jnp.where(places < fixed, places, shifted)]].set(jnp.asarray(lengths, jnp.int32))

    lengths = jnp.where(number % 4 == 0, named(heavy_load, number // 4), named(common, number - number // 4 - 1))
    mixed = jax.random.permutation(jax.random.fold_in(own, 3), number_of)
    source_of, taker = mixed[0:number_of // 2 * 2:2], mixed[1:number_of // 2 * 2:2]
    slack = jnp.minimum(lengths[source_of] - 1, limit - lengths[taker]) // 2
    slack = jnp.where((source_of == order[0]) | (taker == order[0]) | (lengths[taker] == 0), 0, jnp.maximum(slack, 0))
    shifted = jax.random.randint(jax.random.fold_in(own, 4), (number_of // 2,), 0, 1 << 20) % (slack + 1)
    lengths = lengths.at[source_of].add(-shifted).at[taker].add(shifted)
    members = jnp.searchsorted(jnp.cumsum(lengths), jnp.arange(rows * top), side="right").astype(jnp.int32)
    listing = members.reshape(top, rows).T
    listing = listing[jax.random.permutation(jax.random.fold_in(own, 1), rows)]
    rotation = jax.random.randint(jax.random.fold_in(own, 2), (rows, 1), 0, top)
    return jnp.take_along_axis(listing, (jnp.arange(top)[None, :] + rotation) % top, axis=1)


def load_shares(count, total, limit, skew, full):
    weights = [(1 << 20) // math.isqrt(rank ** skew) + 1 for rank in range(1, count + 1)]
    largest = limit if full else min(limit, max(-(-total // count), total * weights[0] // sum(weights)))
    least = 1 if total - largest >= count - 1 else 0
    holding, rest = [largest] + [least] * (count - 1), total - largest - least * (count - 1)
    while rest > 0:
        candidates = [i for i in range(1, count) if holding[i] < largest] or [i for i in range(1, count) if holding[i] < limit]
        mass, budget = sum([weights[i] for i in candidates]), rest
        for i in candidates:
            addition = min(limit - holding[i], max(1, budget * weights[i] // mass), rest)
            holding[i] = holding[i] + addition
            rest = rest - addition
    return np.array(holding)


def gaussian(own_key, extent, scale, reach, shards=(), kind=jnp.bfloat16):
    loudness = block_levels(own_key, extent, shards, -0.22, 0.18) if shards else 1.0
    entries = jax.random.normal(own_key, extent, jnp.float32) * scale * loudness
    return jnp.minimum(jnp.maximum(entries, -reach), reach).astype(kind)


def setup_inputs(seed: int = 0) -> dict:
    key_of = jax.random.split(jax.random.key(seed), 9)
    up_in = gaussian(key_of[0], (SECTIONS, TOKENS, D), 1.0, 6.0, ((0, 16), (1, 16)))
    down_in = gaussian(key_of[1], (SECTIONS, TOKENS, D), 1.0, 6.0, ((0, 16), (1, 16)))
    up_ids_keys = jax.random.split(jax.random.fold_in(key_of[2], 1), SECTIONS * TOKENS // TOK_DEV)
    up_ids_turns = jax.random.permutation(jax.random.fold_in(key_of[2], 3), SECTIONS * TOKENS // TOK_DEV)
    up_ids = jax.vmap(lambda own, number: assign_block(jax.random.fold_in(key_of[2], 2), own, number, TOK_DEV, EXPERTS, TOP, CAP, 2))(up_ids_keys, up_ids_turns).reshape((SECTIONS, TOKENS, TOP))
    down_ids_keys = jax.random.split(jax.random.fold_in(key_of[3], 1), SECTIONS * TOKENS // TOK_DEV)
    down_ids_turns = jax.random.permutation(jax.random.fold_in(key_of[3], 3), SECTIONS * TOKENS // TOK_DEV)
    down_ids = jax.vmap(lambda own, number: assign_block(jax.random.fold_in(key_of[3], 2), own, number, TOK_DEV, EXPERTS, TOP, CAP, 2))(down_ids_keys, down_ids_turns).reshape((SECTIONS, TOKENS, TOP))
    norm_gain = jnp.clip(1.0 + 0.18 * jax.random.normal(key_of[4], (SECTIONS, D), jnp.float32), 0.1, 1.9)
    router = gaussian(key_of[5], (SECTIONS, D, EXPERTS), (D // 4) ** -0.5, 0.25, ((0, 16),))
    w_up = gaussian(key_of[6], (SECTIONS, EXPERTS, D, FFW), D ** -0.5, 0.125, ((0, 16), (1, 16)))
    w_down = gaussian(key_of[7], (SECTIONS, EXPERTS, FFW, D), (FFW // 4) ** -0.5, 0.375, ((0, 16), (1, 16)))
    return {"up_in": up_in, "down_in": down_in, "up_ids": up_ids, "down_ids": down_ids, "norm_gain": norm_gain, "router": router, "w_up": w_up, "w_down": w_down}


def norm_route(x, ids, gain, table):
    xf = x.astype(jnp.float32)
    normed = (xf * lax.rsqrt(lax.optimization_barrier(jnp.mean(xf * xf, axis=-1, keepdims=True)) + 1e-06) * gain).astype(jnp.bfloat16)
    logits = jnp.dot(normed, table, preferred_element_type=jnp.float32)
    chosen = jnp.take_along_axis(logits, ids, axis=1)
    score = jax.nn.sigmoid(chosen)
    gates = score / lax.optimization_barrier(jnp.sum(score, axis=-1, keepdims=True))
    return (normed, gates)

def one_expert(packed):
    rows, up_w, down_w = packed
    up_h = jnp.dot(rows, up_w, preferred_element_type=jnp.float32)
    hidden = jax.nn.silu(up_h).astype(jnp.bfloat16)
    return jnp.dot(hidden, down_w, preferred_element_type=jnp.float32).astype(jnp.bfloat16)

def moe_layer(x, ids, gain, table, up_w, down_w):
    normed, gates = norm_route(x, ids, gain, table)
    blocks = N_EXPERT
    per_block = ids.reshape(blocks, TOK_DEV * TOP)
    onehot = (per_block[:, :, None] == jnp.arange(EXPERTS, dtype=jnp.int32)[None, None, :]).astype(jnp.int32)
    before = jnp.cumsum(onehot, axis=1) - onehot
    slot = lax.optimization_barrier(jnp.sum(before * onehot, axis=-1))
    source = jnp.arange(blocks, dtype=jnp.int32)[:, None]
    target = (per_block * (blocks * CAP) + source * CAP + slot).reshape(-1).astype(jnp.int32)
    repeated = jnp.repeat(normed, TOP, axis=0)
    buffer = jnp.zeros((EXPERTS * blocks * CAP, D), jnp.bfloat16).at[target].set(repeated)
    outputs = lax.map(one_expert, (buffer.reshape(EXPERTS, blocks * CAP, D), up_w, down_w))
    picked = jnp.take(outputs.reshape(EXPERTS * blocks * CAP, D), target, axis=0)
    picked = picked.reshape(TOKENS, TOP, D).astype(jnp.float32)
    combined = lax.optimization_barrier(jnp.sum(gates[:, :, None] * picked, axis=1))
    return (x.astype(jnp.float32) + 2.5 * combined).astype(jnp.bfloat16)

def one_section(packed):
    x_up, ids_up, x_down, ids_down, gain, table, up_w, down_w = packed
    out_up = moe_layer(x_up, ids_up, gain, table, up_w, down_w)
    out_down = moe_layer(x_down, ids_down, gain, table, up_w, down_w)
    return (out_up, out_down)

def reference(up_in, down_in, up_ids, down_ids, norm_gain, router, w_up, w_down):
    layer_up, layer_down = lax.map(one_section, (up_in, up_ids, down_in, down_ids, norm_gain, router, w_up, w_down))
    return (jnp.roll(layer_up, 1, axis=0), jnp.roll(layer_down, -1, axis=0))
```

```python
import jax
import jax.numpy as jnp
from jax import lax
from jax.sharding import PartitionSpec as P

CAP = 32


def shifted(block, axis, distance):
    devices = range(lax.axis_size(axis))
    route = [((i - distance) % len(devices), i) for i in devices]
    return lax.ppermute(block, axis, route)


def layer_route(x, ids, gain, table):
    tokens_here = x.shape[0]
    experts = table.shape[1]
    choose = ids.shape[1]
    xf = x.astype(jnp.float32)
    normed = (xf * lax.rsqrt(jnp.mean(xf * xf, axis=-1, keepdims=True) + 1e-06) * gain).astype(
        jnp.bfloat16
    )
    logits = jnp.dot(normed, table, preferred_element_type=jnp.float32)
    chosen = jnp.take_along_axis(logits, ids, axis=1)
    score = jax.nn.sigmoid(chosen)
    gates = score / jnp.sum(score, axis=-1, keepdims=True)
    onehot = (ids[:, :, None] == jnp.arange(experts, dtype=jnp.int32)[None, None, :]).astype(
        jnp.int32
    )
    flat = onehot.reshape(tokens_here * choose, experts)
    before = jnp.cumsum(flat, axis=0) - flat
    slot = jnp.sum(before * flat, axis=-1).reshape(tokens_here, choose)
    target = ids * CAP + slot
    rows = jnp.arange(experts * CAP, dtype=jnp.int32)
    hit = target[:, :, None] == rows[None, None, :]
    place = jnp.any(hit, axis=1).astype(jnp.bfloat16)
    send = lax.dot_general(
        place, normed, (((0,), (0,)), ((), ())), preferred_element_type=jnp.float32
    ).astype(jnp.bfloat16)
    weight = jnp.sum(jnp.where(hit, gates[:, :, None], 0.0), axis=1)
    weight_hi = weight.astype(jnp.bfloat16)
    weight_lo = (weight - weight_hi.astype(jnp.float32)).astype(jnp.bfloat16)
    return (send, weight_hi, weight_lo)


def apply_experts(rows, up_w, down_w):
    up_h = jnp.dot(rows, up_w, preferred_element_type=jnp.float32)
    hidden = jax.nn.silu(up_h).astype(jnp.bfloat16)
    return jnp.dot(hidden, down_w, preferred_element_type=jnp.float32).astype(jnp.bfloat16)


def finish(x, weight_hi, weight_lo, returned):
    combined = jnp.dot(weight_hi, returned, preferred_element_type=jnp.float32) + jnp.dot(
        weight_lo, returned, preferred_element_type=jnp.float32
    )
    return (x.astype(jnp.float32) + 2.5 * combined).astype(jnp.bfloat16)


def exchange(block):
    return lax.all_to_all(block, "expert", split_axis=0, concat_axis=0, tiled=True)


def per_device(up_in, down_in, up_ids, down_ids, norm_gain, router, w_up, w_down):
    gain = norm_gain[0]
    table = router[0]
    up_w = w_up[0, 0]
    down_w = w_down[0, 0]
    send_up, hi_up, lo_up = layer_route(up_in[0], up_ids[0], gain, table)
    send_down, hi_down, lo_down = layer_route(down_in[0], down_ids[0], gain, table)
    rows_up = exchange(send_up)
    rows_down = exchange(send_down)
    back_up = exchange(apply_experts(rows_up, up_w, down_w))
    back_down = exchange(apply_experts(rows_down, up_w, down_w))
    layer_up = finish(up_in[0], hi_up, lo_up, back_up)
    up_out = shifted(layer_up[None], "pipe", 1)
    layer_down = finish(down_in[0], hi_down, lo_down, back_down)
    down_out = shifted(layer_down[None], "pipe", -1)
    return (up_out, down_out)


def solution(mesh):
    placed = (
        P("pipe", "expert", None),
        P("pipe", "expert", None),
        P("pipe", "expert", None),
        P("pipe", "expert", None),
        P("pipe", None),
        P("pipe", None, None),
        P("pipe", "expert", None, None),
        P("pipe", "expert", None, None),
    )
    return jax.shard_map(
        per_device,
        mesh=mesh,
        in_specs=placed,
        out_specs=(P("pipe", "expert", None), P("pipe", "expert", None)),
        check_vma=False,
    )
```

```python
import jax
import jax.numpy as jnp
from jax import lax
from jax.sharding import PartitionSpec as P

CAP = 32


def shifted(block, axis, distance):
    devices = range(lax.axis_size(axis))
    route = [((i - distance) % len(devices), i) for i in devices]
    return lax.ppermute(block, axis, route)


def layer_route(x, ids, gain, table):
    tokens_here = x.shape[0]
    experts = table.shape[1]
    choose = ids.shape[1]
    xf = x.astype(jnp.float32)
    normed = (xf * lax.rsqrt(jnp.mean(xf * xf, axis=-1, keepdims=True) + 1e-06) * gain).astype(
        jnp.bfloat16
    )
    normed = lax.optimization_barrier(normed)
    logits = jnp.dot(normed, table, preferred_element_type=jnp.float32)
    picks = ids[:, :, None] == jnp.arange(experts, dtype=jnp.int32)[None, None, :]
    chosen = jnp.sum(jnp.where(picks, logits[:, None, :], 0.0), axis=-1)
    score = jax.nn.sigmoid(chosen)
    gates = score / jnp.sum(score, axis=-1, keepdims=True)
    onehot = picks.astype(jnp.int32)
    flat = onehot.reshape(tokens_here * choose, experts)
    before = jnp.cumsum(flat, axis=0) - flat
    slot = jnp.sum(before * flat, axis=-1).reshape(tokens_here, choose)
    target = ids * CAP + slot
    rows = jnp.arange(experts * CAP, dtype=jnp.int32)
    hit = target[:, :, None] == rows[None, None, :]
    place = jnp.any(hit, axis=1).astype(jnp.bfloat16)
    send = lax.dot_general(
        place, normed, (((0,), (0,)), ((), ())), preferred_element_type=jnp.float32
    ).astype(jnp.bfloat16)
    weight = jnp.sum(jnp.where(hit, gates[:, :, None], 0.0), axis=1)
    weight_hi = weight.astype(jnp.bfloat16)
    weight_lo = (weight - weight_hi.astype(jnp.float32)).astype(jnp.bfloat16)
    return (send, weight_hi, weight_lo)


def apply_experts(rows, up_w, down_w):
    up_h = jnp.dot(rows, up_w, preferred_element_type=jnp.float32)
    hidden = jax.nn.silu(up_h).astype(jnp.bfloat16)
    return jnp.dot(hidden, down_w, preferred_element_type=jnp.float32).astype(jnp.bfloat16)


def finish(x, weight_hi, weight_lo, returned):
    combined = jnp.dot(weight_hi, returned, preferred_element_type=jnp.float32) + jnp.dot(
        weight_lo, returned, preferred_element_type=jnp.float32
    )
    return (x.astype(jnp.float32) + 2.5 * combined).astype(jnp.bfloat16)


def exchange(block):
    return lax.all_to_all(block, "expert", split_axis=0, concat_axis=0, tiled=True)


def per_device(up_in, down_in, up_ids, down_ids, norm_gain, router, w_up, w_down):
    gain = norm_gain[0]
    table = router[0]
    up_w = w_up[0, 0]
    down_w = w_down[0, 0]
    send_up, hi_up, lo_up = layer_route(up_in[0], up_ids[0], gain, table)
    send_down, hi_down, lo_down = layer_route(down_in[0], down_ids[0], gain, table)
    rows_up = exchange(send_up)
    rows_down = exchange(send_down)
    back_up = exchange(apply_experts(rows_up, up_w, down_w))
    out_down = apply_experts(rows_down, up_w, down_w)
    layer_up = finish(up_in[0], hi_up, lo_up, back_up)
    layer_up, out_down = lax.optimization_barrier((layer_up, out_down))
    up_out = shifted(layer_up[None], "pipe", 1)
    back_down = exchange(out_down)
    layer_down = finish(down_in[0], hi_down, lo_down, back_down)
    down_out = shifted(layer_down[None], "pipe", -1)
    return (up_out, down_out)


def solution(mesh):
    placed = (
        P("pipe", "expert", None),
        P("pipe", "expert", None),
        P("pipe", "expert", None),
        P("pipe", "expert", None),
        P("pipe", None),
        P("pipe", None, None),
        P("pipe", "expert", None, None),
        P("pipe", "expert", None, None),
    )
    return jax.shard_map(
        per_device,
        mesh=mesh,
        in_specs=placed,
        out_specs=(P("pipe", "expert", None), P("pipe", "expert", None)),
        check_vma=False,
    )
```

```python
import jax
import jax.numpy as jnp
from jax import lax
from jax.sharding import PartitionSpec as P

CAP = 32


def shifted(block, axis, distance):
    devices = range(lax.axis_size(axis))
    route = [((i - distance) % len(devices), i) for i in devices]
    return lax.ppermute(block, axis, route)


def layer_route(x, ids, gain, table):
    tokens_here = x.shape[0]
    experts = table.shape[1]
    choose = ids.shape[1]
    xf = x.astype(jnp.float32)
    normed = (xf * lax.rsqrt(jnp.mean(xf * xf, axis=-1, keepdims=True) + 1e-06) * gain).astype(
        jnp.bfloat16
    )
    normed = lax.optimization_barrier(normed)
    logits = jnp.dot(normed, table, preferred_element_type=jnp.float32)
    picks = ids[:, :, None] == jnp.arange(experts, dtype=jnp.int32)[None, None, :]
    chosen = jnp.sum(jnp.where(picks, logits[:, None, :], 0.0), axis=-1)
    score = jax.nn.sigmoid(chosen)
    gates = score / jnp.sum(score, axis=-1, keepdims=True)
    onehot = picks.astype(jnp.int32)
    flat = onehot.reshape(tokens_here * choose, experts)
    before = jnp.cumsum(flat, axis=0) - flat
    slot = jnp.sum(before * flat, axis=-1).reshape(tokens_here, choose)
    target = ids * CAP + slot
    rows = jnp.arange(experts * CAP, dtype=jnp.int32)
    hit = target[:, :, None] == rows[None, None, :]
    place = jnp.any(hit, axis=1).astype(jnp.bfloat16)
    send = lax.dot_general(
        place, normed, (((0,), (0,)), ((), ())), preferred_element_type=jnp.float32
    ).astype(jnp.bfloat16)
    weight = jnp.sum(jnp.where(hit, gates[:, :, None], 0.0), axis=1)
    weight_hi = weight.astype(jnp.bfloat16)
    weight_lo = (weight - weight_hi.astype(jnp.float32)).astype(jnp.bfloat16)
    return (send, weight_hi, weight_lo)


def apply_experts(rows, up_w, down_w):
    up_h = jnp.dot(rows, up_w, preferred_element_type=jnp.float32)
    hidden = jax.nn.silu(up_h).astype(jnp.bfloat16)
    return jnp.dot(hidden, down_w, preferred_element_type=jnp.float32).astype(jnp.bfloat16)


def finish(x, weight_hi, weight_lo, returned):
    combined = jnp.dot(weight_hi, returned, preferred_element_type=jnp.float32) + jnp.dot(
        weight_lo, returned, preferred_element_type=jnp.float32
    )
    return (x.astype(jnp.float32) + 2.5 * combined).astype(jnp.bfloat16)


def exchange(block):
    return lax.all_to_all(block, "expert", split_axis=0, concat_axis=0, tiled=True)


def per_device(up_in, down_in, up_ids, down_ids, norm_gain, router, w_up, w_down):
    gain = norm_gain[0]
    table = router[0]
    up_w = w_up[0, 0]
    down_w = w_down[0, 0]
    send_up, hi_up, lo_up = layer_route(up_in[0], up_ids[0], gain, table)
    send_down, hi_down, lo_down = layer_route(down_in[0], down_ids[0], gain, table)
    rows_up = exchange(send_up)
    rows_down = exchange(send_down)
    back_up = exchange(apply_experts(rows_up, up_w, down_w))
    back_down = exchange(apply_experts(rows_down, up_w, down_w))
    layer_up = finish(up_in[0], hi_up, lo_up, back_up)
    layer_up, back_down = lax.optimization_barrier((layer_up, back_down))
    up_out = shifted(layer_up[None], "pipe", 1)
    layer_down = finish(down_in[0], hi_down, lo_down, back_down)
    down_out = shifted(layer_down[None], "pipe", -1)
    return (up_out, down_out)


def solution(mesh):
    placed = (
        P("pipe", "expert", None),
        P("pipe", "expert", None),
        P("pipe", "expert", None),
        P("pipe", "expert", None),
        P("pipe", None),
        P("pipe", None, None),
        P("pipe", "expert", None, None),
        P("pipe", "expert", None, None),
    )
    return jax.shard_map(
        per_device,
        mesh=mesh,
        in_specs=placed,
        out_specs=(P("pipe", "expert", None), P("pipe", "expert", None)),
        check_vma=False,
    )
```

```python
import jax
import jax.numpy as jnp
from jax import lax
from jax.sharding import PartitionSpec as P

CAP = 32


def shifted(block, axis, distance):
    devices = range(lax.axis_size(axis))
    route = [((i - distance) % len(devices), i) for i in devices]
    return lax.ppermute(block, axis, route)


def layer_route(x, ids, gain, table):
    tokens_here = x.shape[0]
    experts = table.shape[1]
    choose = ids.shape[1]
    xf = x.astype(jnp.float32)
    normed = (xf * lax.rsqrt(jnp.mean(xf * xf, axis=-1, keepdims=True) + 1e-06) * gain).astype(
        jnp.bfloat16
    )
    normed = lax.optimization_barrier(normed)
    logits = jnp.dot(normed, table, preferred_element_type=jnp.float32)
    picks = ids[:, :, None] == jnp.arange(experts, dtype=jnp.int32)[None, None, :]
    chosen = jnp.sum(jnp.where(picks, logits[:, None, :], 0.0), axis=-1)
    score = jax.nn.sigmoid(chosen)
    gates = score / jnp.sum(score, axis=-1, keepdims=True)
    onehot = picks.astype(jnp.int32)
    flat = onehot.reshape(tokens_here * choose, experts)
    before = jnp.cumsum(flat, axis=0) - flat
    slot = jnp.sum(before * flat, axis=-1).reshape(tokens_here, choose)
    target = ids * CAP + slot
    rows = jnp.arange(experts * CAP, dtype=jnp.int32)
    hit = target[:, :, None] == rows[None, None, :]
    place = jnp.any(hit, axis=1).astype(jnp.bfloat16)
    send = lax.dot_general(
        place, normed, (((0,), (0,)), ((), ())), preferred_element_type=jnp.float32
    ).astype(jnp.bfloat16)
    weight = jnp.sum(jnp.where(hit, gates[:, :, None], 0.0), axis=1)
    weight_hi = weight.astype(jnp.bfloat16)
    weight_lo = (weight - weight_hi.astype(jnp.float32)).astype(jnp.bfloat16)
    return (send, weight_hi, weight_lo)


def apply_experts(rows, up_w, down_w):
    up_h = jnp.dot(rows, up_w, preferred_element_type=jnp.float32)
    hidden = jax.nn.silu(up_h).astype(jnp.bfloat16)
    return jnp.dot(hidden, down_w, preferred_element_type=jnp.float32).astype(jnp.bfloat16)


def finish(x, weight_hi, weight_lo, returned):
    combined = jnp.dot(weight_hi, returned, preferred_element_type=jnp.float32) + jnp.dot(
        weight_lo, returned, preferred_element_type=jnp.float32
    )
    return (x.astype(jnp.float32) + 2.5 * combined).astype(jnp.bfloat16)


def exchange(block):
    return lax.all_to_all(block, "expert", split_axis=0, concat_axis=0, tiled=True)


def per_device(up_in, down_in, up_ids, down_ids, norm_gain, router, w_up, w_down):
    gain = norm_gain[0]
    table = router[0]
    up_w = w_up[0, 0]
    down_w = w_down[0, 0]
    send_up, hi_up, lo_up = layer_route(up_in[0], up_ids[0], gain, table)
    send_up, x_down, ids_down = lax.optimization_barrier((send_up, down_in[0], down_ids[0]))
    send_down, hi_down, lo_down = layer_route(x_down, ids_down, gain, table)
    rows_up = exchange(send_up)
    rows_down = exchange(send_down)
    back_up = exchange(apply_experts(rows_up, up_w, down_w))
    back_down = exchange(apply_experts(rows_down, up_w, down_w))
    layer_up = finish(up_in[0], hi_up, lo_up, back_up)
    up_out = shifted(layer_up[None], "pipe", 1)
    layer_down = finish(x_down, hi_down, lo_down, back_down)
    down_out = shifted(layer_down[None], "pipe", -1)
    return (up_out, down_out)


def solution(mesh):
    placed = (
        P("pipe", "expert", None),
        P("pipe", "expert", None),
        P("pipe", "expert", None),
        P("pipe", "expert", None),
        P("pipe", None),
        P("pipe", None, None),
        P("pipe", "expert", None, None),
        P("pipe", "expert", None, None),
    )
    return jax.shard_map(
        per_device,
        mesh=mesh,
        in_specs=placed,
        out_specs=(P("pipe", "expert", None), P("pipe", "expert", None)),
        check_vma=False,
    )
```

```python
import jax
import jax.numpy as jnp
from jax import lax
from jax.sharding import PartitionSpec as P

CAP = 32


def shifted(block, axis, distance):
    devices = range(lax.axis_size(axis))
    route = [((i - distance) % len(devices), i) for i in devices]
    return lax.ppermute(block, axis, route)


def layer_route(x, ids, gain, table):
    tokens_here = x.shape[0]
    experts = table.shape[1]
    choose = ids.shape[1]
    xf = x.astype(jnp.float32)
    normed = (xf * lax.rsqrt(jnp.mean(xf * xf, axis=-1, keepdims=True) + 1e-06) * gain).astype(
        jnp.bfloat16
    )
    normed = lax.optimization_barrier(normed)
    logits = jnp.dot(normed, table, preferred_element_type=jnp.float32)
    picks = ids[:, :, None] == jnp.arange(experts, dtype=jnp.int32)[None, None, :]
    chosen = jnp.sum(jnp.where(picks, logits[:, None, :], 0.0), axis=-1)
    score = jax.nn.sigmoid(chosen)
    gates = score / jnp.sum(score, axis=-1, keepdims=True)
    onehot = picks.astype(jnp.int32)
    flat = onehot.reshape(tokens_here * choose, experts)
    before = jnp.cumsum(flat, axis=0) - flat
    slot = jnp.sum(before * flat, axis=-1).reshape(tokens_here, choose)
    target = ids * CAP + slot
    rows = jnp.arange(experts * CAP, dtype=jnp.int32)
    hit = target[:, :, None] == rows[None, None, :]
    place = jnp.any(hit, axis=1).astype(jnp.bfloat16)
    send = lax.dot_general(
        place, normed, (((0,), (0,)), ((), ())), preferred_element_type=jnp.float32
    ).astype(jnp.bfloat16)
    weight = jnp.sum(jnp.where(hit, gates[:, :, None], 0.0), axis=1)
    weight_hi = weight.astype(jnp.bfloat16)
    weight_lo = (weight - weight_hi.astype(jnp.float32)).astype(jnp.bfloat16)
    return (send, weight_hi, weight_lo)


def apply_experts(rows, up_w, down_w):
    up_h = jnp.dot(rows, up_w, preferred_element_type=jnp.float32)
    hidden = jax.nn.silu(up_h).astype(jnp.bfloat16)
    return jnp.dot(hidden, down_w, preferred_element_type=jnp.float32).astype(jnp.bfloat16)


def finish(x, weight_hi, weight_lo, returned):
    combined = jnp.dot(weight_hi, returned, preferred_element_type=jnp.float32) + jnp.dot(
        weight_lo, returned, preferred_element_type=jnp.float32
    )
    return (x.astype(jnp.float32) + 2.5 * combined).astype(jnp.bfloat16)


def exchange(block):
    return lax.all_to_all(block, "expert", split_axis=0, concat_axis=0, tiled=True)


def per_device(up_in, down_in, up_ids, down_ids, norm_gain, router, w_up, w_down):
    gain = norm_gain[0]
    table = router[0]
    up_w = w_up[0, 0]
    down_w = w_down[0, 0]
    send_up, hi_up, lo_up = layer_route(up_in[0], up_ids[0], gain, table)
    send_down, hi_down, lo_down = layer_route(down_in[0], down_ids[0], gain, table)
    owners = lax.axis_size("expert")
    width = send_up.shape[-1]
    both = jnp.stack(
        [send_up.reshape(owners, -1, width), send_down.reshape(owners, -1, width)], axis=1
    )
    arrived = exchange(both.reshape(-1, width)).reshape(owners, 2, -1, width)
    rows_up = arrived[:, 0].reshape(-1, width)
    rows_down = arrived[:, 1].reshape(-1, width)
    back_up = exchange(apply_experts(rows_up, up_w, down_w))
    back_down = exchange(apply_experts(rows_down, up_w, down_w))
    layer_up = finish(up_in[0], hi_up, lo_up, back_up)
    up_out = shifted(layer_up[None], "pipe", 1)
    layer_down = finish(down_in[0], hi_down, lo_down, back_down)
    down_out = shifted(layer_down[None], "pipe", -1)
    return (up_out, down_out)


def solution(mesh):
    placed = (
        P("pipe", "expert", None),
        P("pipe", "expert", None),
        P("pipe", "expert", None),
        P("pipe", "expert", None),
        P("pipe", None),
        P("pipe", None, None),
        P("pipe", "expert", None, None),
        P("pipe", "expert", None, None),
    )
    return jax.shard_map(
        per_device,
        mesh=mesh,
        in_specs=placed,
        out_specs=(P("pipe", "expert", None), P("pipe", "expert", None)),
        check_vma=False,
    )
```

```python
import jax
import jax.numpy as jnp
from jax import lax
from jax.sharding import PartitionSpec as P

CAP = 32


def shifted(block, axis, distance):
    devices = range(lax.axis_size(axis))
    route = [((i - distance) % len(devices), i) for i in devices]
    return lax.ppermute(block, axis, route)


def layer_route(x, ids, gain, table):
    tokens_here = x.shape[0]
    experts = table.shape[1]
    choose = ids.shape[1]
    xf = x.astype(jnp.float32)
    normed = (xf * lax.rsqrt(jnp.mean(xf * xf, axis=-1, keepdims=True) + 1e-06) * gain).astype(
        jnp.bfloat16
    )
    normed = lax.optimization_barrier(normed)
    logits = jnp.dot(normed, table, preferred_element_type=jnp.float32)
    picks = ids[:, :, None] == jnp.arange(experts, dtype=jnp.int32)[None, None, :]
    chosen = jnp.sum(jnp.where(picks, logits[:, None, :], 0.0), axis=-1)
    score = jax.nn.sigmoid(chosen)
    gates = score / jnp.sum(score, axis=-1, keepdims=True)
    onehot = picks.astype(jnp.int32)
    flat = onehot.reshape(tokens_here * choose, experts)
    before = jnp.cumsum(flat, axis=0) - flat
    slot = jnp.sum(before * flat, axis=-1).reshape(tokens_here, choose)
    target = ids * CAP + slot
    rows = jnp.arange(experts * CAP, dtype=jnp.int32)
    hit = target[:, :, None] == rows[None, None, :]
    place = jnp.any(hit, axis=1).astype(jnp.bfloat16)
    send = lax.dot_general(
        place, normed, (((0,), (0,)), ((), ())), preferred_element_type=jnp.float32
    ).astype(jnp.bfloat16)
    weight = jnp.sum(jnp.where(hit, gates[:, :, None], 0.0), axis=1)
    weight_hi = weight.astype(jnp.bfloat16)
    weight_lo = (weight - weight_hi.astype(jnp.float32)).astype(jnp.bfloat16)
    return (send, weight_hi, weight_lo)


def apply_experts(rows, up_w, down_w):
    up_h = jnp.dot(rows, up_w, preferred_element_type=jnp.float32)
    hidden = jax.nn.silu(up_h).astype(jnp.bfloat16)
    return jnp.dot(hidden, down_w, preferred_element_type=jnp.float32).astype(jnp.bfloat16)


def finish(x, weight_hi, weight_lo, returned):
    combined = jnp.dot(weight_hi, returned, preferred_element_type=jnp.float32) + jnp.dot(
        weight_lo, returned, preferred_element_type=jnp.float32
    )
    return (x.astype(jnp.float32) + 2.5 * combined).astype(jnp.bfloat16)


def exchange(block):
    return lax.all_to_all(block, "expert", split_axis=0, concat_axis=0, tiled=True)


def per_device(up_in, down_in, up_ids, down_ids, norm_gain, router, w_up, w_down):
    gain = norm_gain[0]
    table = router[0]
    up_w = w_up[0, 0]
    down_w = w_down[0, 0]
    send_up, hi_up, lo_up = layer_route(up_in[0], up_ids[0], gain, table)
    send_down, hi_down, lo_down = layer_route(down_in[0], down_ids[0], gain, table)
    owners = lax.axis_size("expert")
    width = send_up.shape[-1]
    both = jnp.stack(
        [send_up.reshape(owners, -1, width), send_down.reshape(owners, -1, width)], axis=1
    )
    arrived = exchange(both.reshape(-1, width))
    back = exchange(apply_experts(arrived, up_w, down_w)).reshape(owners, 2, -1, width)
    back_up = back[:, 0].reshape(-1, width)
    back_down = back[:, 1].reshape(-1, width)
    layer_up = finish(up_in[0], hi_up, lo_up, back_up)
    up_out = shifted(layer_up[None], "pipe", 1)
    layer_down = finish(down_in[0], hi_down, lo_down, back_down)
    down_out = shifted(layer_down[None], "pipe", -1)
    return (up_out, down_out)


def solution(mesh):
    placed = (
        P("pipe", "expert", None),
        P("pipe", "expert", None),
        P("pipe", "expert", None),
        P("pipe", "expert", None),
        P("pipe", None),
        P("pipe", None, None),
        P("pipe", "expert", None, None),
        P("pipe", "expert", None, None),
    )
    return jax.shard_map(
        per_device,
        mesh=mesh,
        in_specs=placed,
        out_specs=(P("pipe", "expert", None), P("pipe", "expert", None)),
        check_vma=False,
    )
```

```python
import jax
import jax.numpy as jnp
from jax import lax
from jax.experimental import pallas as pl
from jax.sharding import PartitionSpec as P

CAP = 32

def dispatch_kernel(x_ref, gain_ref, ids_ref, send_ref, normed_ref):
    tokens, width = x_ref.shape
    rows = send_ref.shape[0]
    xf = x_ref[...].astype(jnp.float32)
    ms = jnp.mean(xf * xf, axis=-1, keepdims=True)
    normed = (xf * lax.rsqrt(ms + 1e-06) * gain_ref[...]).astype(jnp.bfloat16)
    normed_ref[...] = normed
    ids = ids_ref[...]
    owner = lax.broadcasted_iota(jnp.int32, (tokens, rows), 1) // CAP
    member = ids[:, 0:1] == owner
    for k in range(1, ids.shape[1]):
        member = member | (ids[:, k:k + 1] == owner)
    member = member.astype(jnp.float32)
    earlier = (lax.broadcasted_iota(jnp.int32, (tokens, tokens), 1)
               < lax.broadcasted_iota(jnp.int32, (tokens, tokens), 0)).astype(jnp.bfloat16)
    slot = jnp.dot(earlier, member.astype(jnp.bfloat16), preferred_element_type=jnp.float32)
    offset = (lax.broadcasted_iota(jnp.int32, (tokens, rows), 1) % CAP).astype(jnp.float32)
    place = jnp.where(slot == offset, member, 0.0)
    place_t = place.T.astype(jnp.bfloat16)
    send_ref[...] = jnp.dot(place_t, normed, preferred_element_type=jnp.float32).astype(jnp.bfloat16)

def dispatch(x, gain, ids, experts):
    tokens, width = x.shape
    rows = experts * CAP
    return pl.pallas_call(
        dispatch_kernel,
        out_shape=(jax.ShapeDtypeStruct((rows, width), jnp.bfloat16),
                   jax.ShapeDtypeStruct((tokens, width), jnp.bfloat16)),
    )(x, gain.reshape(1, width), ids)


def shifted(block, axis, distance):
    devices = range(lax.axis_size(axis))
    route = [((i - distance) % len(devices), i) for i in devices]
    return lax.ppermute(block, axis, route)


def layer_route(x, ids, gain, table):
    tokens_here = x.shape[0]
    experts = table.shape[1]
    choose = ids.shape[1]
    send, normed = dispatch(x, gain, ids, experts)
    logits = jnp.dot(normed, table, preferred_element_type=jnp.float32)
    chosen = jnp.take_along_axis(logits, ids, axis=1)
    score = jax.nn.sigmoid(chosen)
    gates = score / jnp.sum(score, axis=-1, keepdims=True)
    onehot = (ids[:, :, None] == jnp.arange(experts, dtype=jnp.int32)[None, None, :]).astype(
        jnp.int32
    )
    flat = onehot.reshape(tokens_here * choose, experts)
    before = jnp.cumsum(flat, axis=0) - flat
    slot = jnp.sum(before * flat, axis=-1).reshape(tokens_here, choose)
    target = ids * CAP + slot
    rows = jnp.arange(experts * CAP, dtype=jnp.int32)
    hit = target[:, :, None] == rows[None, None, :]
    weight = jnp.sum(jnp.where(hit, gates[:, :, None], 0.0), axis=1)
    weight_hi = weight.astype(jnp.bfloat16)
    weight_lo = (weight - weight_hi.astype(jnp.float32)).astype(jnp.bfloat16)
    return (send, weight_hi, weight_lo)


def apply_experts(rows, up_w, down_w):
    up_h = jnp.dot(rows, up_w, preferred_element_type=jnp.float32)
    hidden = jax.nn.silu(up_h).astype(jnp.bfloat16)
    return jnp.dot(hidden, down_w, preferred_element_type=jnp.float32).astype(jnp.bfloat16)


def finish(x, weight_hi, weight_lo, returned):
    combined = jnp.dot(weight_hi, returned, preferred_element_type=jnp.float32) + jnp.dot(
        weight_lo, returned, preferred_element_type=jnp.float32
    )
    return (x.astype(jnp.float32) + 2.5 * combined).astype(jnp.bfloat16)


def exchange(block):
    return lax.all_to_all(block, "expert", split_axis=0, concat_axis=0, tiled=True)


def per_device(up_in, down_in, up_ids, down_ids, norm_gain, router, w_up, w_down):
    gain = norm_gain[0]
    table = router[0]
    up_w = w_up[0, 0]
    down_w = w_down[0, 0]
    send_up, hi_up, lo_up = layer_route(up_in[0], up_ids[0], gain, table)
    send_down, hi_down, lo_down = layer_route(down_in[0], down_ids[0], gain, table)
    rows_up = exchange(send_up)
    rows_down = exchange(send_down)
    back_up = exchange(apply_experts(rows_up, up_w, down_w))
    back_down = exchange(apply_experts(rows_down, up_w, down_w))
    layer_up = finish(up_in[0], hi_up, lo_up, back_up)
    up_out = shifted(layer_up[None], "pipe", 1)
    layer_down = finish(down_in[0], hi_down, lo_down, back_down)
    down_out = shifted(layer_down[None], "pipe", -1)
    return (up_out, down_out)


def solution(mesh):
    placed = (
        P("pipe", "expert", None),
        P("pipe", "expert", None),
        P("pipe", "expert", None),
        P("pipe", "expert", None),
        P("pipe", None),
        P("pipe", None, None),
        P("pipe", "expert", None, None),
        P("pipe", "expert", None, None),
    )
    return jax.shard_map(
        per_device,
        mesh=mesh,
        in_specs=placed,
        out_specs=(P("pipe", "expert", None), P("pipe", "expert", None)),
        check_vma=False,
    )
```

```python
import jax
import jax.numpy as jnp
from jax import lax
from jax.experimental import pallas as pl
from jax.sharding import PartitionSpec as P

CAP = 32

def dispatch_kernel(x_ref, gain_ref, ids_ref, send_ref, normed_ref):
    step = pl.program_id(0)
    tokens = x_ref.shape[0]
    block = send_ref.shape[0]

    @pl.when(step == 0)
    def _():
        xf = x_ref[...].astype(jnp.float32)
        ms = jnp.mean(xf * xf, axis=-1, keepdims=True)
        normed_ref[...] = (xf * lax.rsqrt(ms + 1e-06) * gain_ref[...]).astype(jnp.bfloat16)

    ids = ids_ref[...]
    row = lax.broadcasted_iota(jnp.int32, (tokens, block), 1) + step * block
    owner = row // CAP
    member = ids[:, 0:1] == owner
    for k in range(1, ids.shape[1]):
        member = member | (ids[:, k:k + 1] == owner)
    member = member.astype(jnp.float32)
    earlier = (lax.broadcasted_iota(jnp.int32, (tokens, tokens), 1)
               < lax.broadcasted_iota(jnp.int32, (tokens, tokens), 0)).astype(jnp.bfloat16)
    slot = jnp.dot(earlier, member.astype(jnp.bfloat16), preferred_element_type=jnp.float32)
    offset = (row % CAP).astype(jnp.float32)
    place = jnp.where(slot == offset, member, 0.0)
    place_t = place.T.astype(jnp.bfloat16)
    send_ref[...] = jnp.dot(
        place_t, normed_ref[...], preferred_element_type=jnp.float32
    ).astype(jnp.bfloat16)


def dispatch(x, gain, ids, experts):
    tokens, width = x.shape
    rows = experts * CAP
    block = 128
    return pl.pallas_call(
        dispatch_kernel,
        grid=(rows // block,),
        in_specs=[
            pl.BlockSpec((tokens, width), lambda i: (0, 0)),
            pl.BlockSpec((1, width), lambda i: (0, 0)),
            pl.BlockSpec((tokens, ids.shape[1]), lambda i: (0, 0)),
        ],
        out_specs=(
            pl.BlockSpec((block, width), lambda i: (i, 0)),
            pl.BlockSpec((tokens, width), lambda i: (0, 0)),
        ),
        out_shape=(jax.ShapeDtypeStruct((rows, width), jnp.bfloat16),
                   jax.ShapeDtypeStruct((tokens, width), jnp.bfloat16)),
    )(x, gain.reshape(1, width), ids)


def shifted(block, axis, distance):
    devices = range(lax.axis_size(axis))
    route = [((i - distance) % len(devices), i) for i in devices]
    return lax.ppermute(block, axis, route)


def layer_route(x, ids, gain, table):
    tokens_here = x.shape[0]
    experts = table.shape[1]
    choose = ids.shape[1]
    send, normed = dispatch(x, gain, ids, experts)
    logits = jnp.dot(normed, table, preferred_element_type=jnp.float32)
    chosen = jnp.take_along_axis(logits, ids, axis=1)
    score = jax.nn.sigmoid(chosen)
    gates = score / jnp.sum(score, axis=-1, keepdims=True)
    onehot = (ids[:, :, None] == jnp.arange(experts, dtype=jnp.int32)[None, None, :]).astype(
        jnp.int32
    )
    flat = onehot.reshape(tokens_here * choose, experts)
    before = jnp.cumsum(flat, axis=0) - flat
    slot = jnp.sum(before * flat, axis=-1).reshape(tokens_here, choose)
    target = ids * CAP + slot
    rows = jnp.arange(experts * CAP, dtype=jnp.int32)
    hit = target[:, :, None] == rows[None, None, :]
    weight = jnp.sum(jnp.where(hit, gates[:, :, None], 0.0), axis=1)
    weight_hi = weight.astype(jnp.bfloat16)
    weight_lo = (weight - weight_hi.astype(jnp.float32)).astype(jnp.bfloat16)
    return (send, weight_hi, weight_lo)


def apply_experts(rows, up_w, down_w):
    up_h = jnp.dot(rows, up_w, preferred_element_type=jnp.float32)
    hidden = jax.nn.silu(up_h).astype(jnp.bfloat16)
    return jnp.dot(hidden, down_w, preferred_element_type=jnp.float32).astype(jnp.bfloat16)


def finish(x, weight_hi, weight_lo, returned):
    combined = jnp.dot(weight_hi, returned, preferred_element_type=jnp.float32) + jnp.dot(
        weight_lo, returned, preferred_element_type=jnp.float32
    )
    return (x.astype(jnp.float32) + 2.5 * combined).astype(jnp.bfloat16)


def exchange(block):
    return lax.all_to_all(block, "expert", split_axis=0, concat_axis=0, tiled=True)


def per_device(up_in, down_in, up_ids, down_ids, norm_gain, router, w_up, w_down):
    gain = norm_gain[0]
    table = router[0]
    up_w = w_up[0, 0]
    down_w = w_down[0, 0]
    send_up, hi_up, lo_up = layer_route(up_in[0], up_ids[0], gain, table)
    send_down, hi_down, lo_down = layer_route(down_in[0], down_ids[0], gain, table)
    rows_up = exchange(send_up)
    rows_down = exchange(send_down)
    back_up = exchange(apply_experts(rows_up, up_w, down_w))
    back_down = exchange(apply_experts(rows_down, up_w, down_w))
    layer_up = finish(up_in[0], hi_up, lo_up, back_up)
    up_out = shifted(layer_up[None], "pipe", 1)
    layer_down = finish(down_in[0], hi_down, lo_down, back_down)
    down_out = shifted(layer_down[None], "pipe", -1)
    return (up_out, down_out)


def solution(mesh):
    placed = (
        P("pipe", "expert", None),
        P("pipe", "expert", None),
        P("pipe", "expert", None),
        P("pipe", "expert", None),
        P("pipe", None),
        P("pipe", None, None),
        P("pipe", "expert", None, None),
        P("pipe", "expert", None, None),
    )
    return jax.shard_map(
        per_device,
        mesh=mesh,
        in_specs=placed,
        out_specs=(P("pipe", "expert", None), P("pipe", "expert", None)),
        check_vma=False,
    )
```

```python
import jax
import jax.numpy as jnp
from jax import lax
from jax.experimental import pallas as pl
from jax.sharding import PartitionSpec as P

CAP = 32

def dispatch_kernel(x_ref, gain_ref, ids_ref, send_ref, normed_ref):
    tokens = x_ref.shape[0]
    rows = send_ref.shape[0]
    xf = x_ref[...].astype(jnp.float32)
    ms = jnp.mean(xf * xf, axis=-1, keepdims=True)
    normed = (xf * lax.rsqrt(ms + 1e-06) * gain_ref[...]).astype(jnp.bfloat16)
    normed_ref[...] = normed
    ids = ids_ref[...]
    row = lax.broadcasted_iota(jnp.int32, (rows, tokens), 0)
    owner = row // CAP
    member = ids[0:1, :] == owner
    for k in range(1, ids.shape[0]):
        member = member | (ids[k:k + 1, :] == owner)
    member = member.astype(jnp.bfloat16)
    later = (lax.broadcasted_iota(jnp.int32, (tokens, tokens), 0)
             < lax.broadcasted_iota(jnp.int32, (tokens, tokens), 1)).astype(jnp.bfloat16)
    slot = jnp.dot(member, later, preferred_element_type=jnp.float32)
    offset = (row % CAP).astype(jnp.float32)
    place = jnp.where(slot == offset, member, jnp.zeros_like(member))
    send_ref[...] = jnp.dot(place, normed, preferred_element_type=jnp.float32).astype(jnp.bfloat16)


def dispatch(x, gain, ids, experts):
    tokens, width = x.shape
    rows = experts * CAP
    return pl.pallas_call(
        dispatch_kernel,
        out_shape=(jax.ShapeDtypeStruct((rows, width), jnp.bfloat16),
                   jax.ShapeDtypeStruct((tokens, width), jnp.bfloat16)),
    )(x, gain.reshape(1, width), ids.T)


def shifted(block, axis, distance):
    devices = range(lax.axis_size(axis))
    route = [((i - distance) % len(devices), i) for i in devices]
    return lax.ppermute(block, axis, route)


def layer_route(x, ids, gain, table):
    tokens_here = x.shape[0]
    experts = table.shape[1]
    choose = ids.shape[1]
    send, normed = dispatch(x, gain, ids, experts)
    logits = jnp.dot(normed, table, preferred_element_type=jnp.float32)
    chosen = jnp.take_along_axis(logits, ids, axis=1)
    score = jax.nn.sigmoid(chosen)
    gates = score / jnp.sum(score, axis=-1, keepdims=True)
    onehot = (ids[:, :, None] == jnp.arange(experts, dtype=jnp.int32)[None, None, :]).astype(
        jnp.int32
    )
    flat = onehot.reshape(tokens_here * choose, experts)
    before = jnp.cumsum(flat, axis=0) - flat
    slot = jnp.sum(before * flat, axis=-1).reshape(tokens_here, choose)
    target = ids * CAP + slot
    rows = jnp.arange(experts * CAP, dtype=jnp.int32)
    hit = target[:, :, None] == rows[None, None, :]
    weight = jnp.sum(jnp.where(hit, gates[:, :, None], 0.0), axis=1)
    weight_hi = weight.astype(jnp.bfloat16)
    weight_lo = (weight - weight_hi.astype(jnp.float32)).astype(jnp.bfloat16)
    return (send, weight_hi, weight_lo)


def apply_experts(rows, up_w, down_w):
    up_h = jnp.dot(rows, up_w, preferred_element_type=jnp.float32)
    hidden = jax.nn.silu(up_h).astype(jnp.bfloat16)
    return jnp.dot(hidden, down_w, preferred_element_type=jnp.float32).astype(jnp.bfloat16)


def finish(x, weight_hi, weight_lo, returned):
    combined = jnp.dot(weight_hi, returned, preferred_element_type=jnp.float32) + jnp.dot(
        weight_lo, returned, preferred_element_type=jnp.float32
    )
    return (x.astype(jnp.float32) + 2.5 * combined).astype(jnp.bfloat16)


def exchange(block):
    return lax.all_to_all(block, "expert", split_axis=0, concat_axis=0, tiled=True)


def per_device(up_in, down_in, up_ids, down_ids, norm_gain, router, w_up, w_down):
    gain = norm_gain[0]
    table = router[0]
    up_w = w_up[0, 0]
    down_w = w_down[0, 0]
    send_up, hi_up, lo_up = layer_route(up_in[0], up_ids[0], gain, table)
    send_down, hi_down, lo_down = layer_route(down_in[0], down_ids[0], gain, table)
    rows_up = exchange(send_up)
    rows_down = exchange(send_down)
    back_up = exchange(apply_experts(rows_up, up_w, down_w))
    back_down = exchange(apply_experts(rows_down, up_w, down_w))
    layer_up = finish(up_in[0], hi_up, lo_up, back_up)
    up_out = shifted(layer_up[None], "pipe", 1)
    layer_down = finish(down_in[0], hi_down, lo_down, back_down)
    down_out = shifted(layer_down[None], "pipe", -1)
    return (up_out, down_out)


def solution(mesh):
    placed = (
        P("pipe", "expert", None),
        P("pipe", "expert", None),
        P("pipe", "expert", None),
        P("pipe", "expert", None),
        P("pipe", None),
        P("pipe", None, None),
        P("pipe", "expert", None, None),
        P("pipe", "expert", None, None),
    )
    return jax.shard_map(
        per_device,
        mesh=mesh,
        in_specs=placed,
        out_specs=(P("pipe", "expert", None), P("pipe", "expert", None)),
        check_vma=False,
    )
```

```python
import jax
import jax.numpy as jnp
from jax import lax
from jax.experimental import pallas as pl
from jax.sharding import PartitionSpec as P

CAP = 32

def dispatch_kernel(x_ref, gain_ref, ids_ref, send_ref, normed_ref):
    tokens = x_ref.shape[0]
    rows = send_ref.shape[0]
    xf = x_ref[...].astype(jnp.float32)
    ms = jnp.mean(xf * xf, axis=-1, keepdims=True)
    normed = (xf * lax.rsqrt(ms + 1e-06) * gain_ref[...]).astype(jnp.bfloat16)
    normed_ref[...] = normed
    row = lax.broadcasted_iota(jnp.int32, (rows, tokens), 0)
    owner = row // CAP
    member = ids_ref[0] == owner
    for k in range(1, ids_ref.shape[0]):
        member = member | (ids_ref[k] == owner)
    member = member.astype(jnp.bfloat16)
    later = (lax.broadcasted_iota(jnp.int32, (tokens, tokens), 0)
             < lax.broadcasted_iota(jnp.int32, (tokens, tokens), 1)).astype(jnp.bfloat16)
    slot = jnp.dot(member, later, preferred_element_type=jnp.float32)
    offset = (row % CAP).astype(jnp.float32)
    place = jnp.where(slot == offset, member, jnp.zeros_like(member))
    send_ref[...] = jnp.dot(place, normed, preferred_element_type=jnp.float32).astype(jnp.bfloat16)


def dispatch(x, gain, ids, experts):
    tokens, width = x.shape
    rows = experts * CAP
    return pl.pallas_call(
        dispatch_kernel,
        out_shape=(jax.ShapeDtypeStruct((rows, width), jnp.bfloat16),
                   jax.ShapeDtypeStruct((tokens, width), jnp.bfloat16)),
    )(x, gain.reshape(1, width), jnp.transpose(ids, (2, 0, 1)))


def shifted(block, axis, distance):
    devices = range(lax.axis_size(axis))
    route = [((i - distance) % len(devices), i) for i in devices]
    return lax.ppermute(block, axis, route)


def layer_route(x, ids_block, gain, table):
    ids = ids_block[0]
    tokens_here = x.shape[0]
    experts = table.shape[1]
    choose = ids.shape[1]
    send, normed = dispatch(x, gain, ids_block, experts)
    logits = jnp.dot(normed, table, preferred_element_type=jnp.float32)
    chosen = jnp.take_along_axis(logits, ids, axis=1)
    score = jax.nn.sigmoid(chosen)
    gates = score / jnp.sum(score, axis=-1, keepdims=True)
    onehot = (ids[:, :, None] == jnp.arange(experts, dtype=jnp.int32)[None, None, :]).astype(
        jnp.int32
    )
    flat = onehot.reshape(tokens_here * choose, experts)
    before = jnp.cumsum(flat, axis=0) - flat
    slot = jnp.sum(before * flat, axis=-1).reshape(tokens_here, choose)
    target = ids * CAP + slot
    rows = jnp.arange(experts * CAP, dtype=jnp.int32)
    hit = target[:, :, None] == rows[None, None, :]
    weight = jnp.sum(jnp.where(hit, gates[:, :, None], 0.0), axis=1)
    weight_hi = weight.astype(jnp.bfloat16)
    weight_lo = (weight - weight_hi.astype(jnp.float32)).astype(jnp.bfloat16)
    return (send, weight_hi, weight_lo)


def apply_experts(rows, up_w, down_w):
    up_h = jnp.dot(rows, up_w, preferred_element_type=jnp.float32)
    hidden = jax.nn.silu(up_h).astype(jnp.bfloat16)
    return jnp.dot(hidden, down_w, preferred_element_type=jnp.float32).astype(jnp.bfloat16)


def finish(x, weight_hi, weight_lo, returned):
    combined = jnp.dot(weight_hi, returned, preferred_element_type=jnp.float32) + jnp.dot(
        weight_lo, returned, preferred_element_type=jnp.float32
    )
    return (x.astype(jnp.float32) + 2.5 * combined).astype(jnp.bfloat16)


def exchange(block):
    return lax.all_to_all(block, "expert", split_axis=0, concat_axis=0, tiled=True)


def per_device(up_in, down_in, up_ids, down_ids, norm_gain, router, w_up, w_down):
    gain = norm_gain[0]
    table = router[0]
    up_w = w_up[0, 0]
    down_w = w_down[0, 0]
    send_up, hi_up, lo_up = layer_route(up_in[0], up_ids, gain, table)
    send_down, hi_down, lo_down = layer_route(down_in[0], down_ids, gain, table)
    rows_up = exchange(send_up)
    rows_down = exchange(send_down)
    back_up = exchange(apply_experts(rows_up, up_w, down_w))
    back_down = exchange(apply_experts(rows_down, up_w, down_w))
    layer_up = finish(up_in[0], hi_up, lo_up, back_up)
    up_out = shifted(layer_up[None], "pipe", 1)
    layer_down = finish(down_in[0], hi_down, lo_down, back_down)
    down_out = shifted(layer_down[None], "pipe", -1)
    return (up_out, down_out)


def solution(mesh):
    placed = (
        P("pipe", "expert", None),
        P("pipe", "expert", None),
        P("pipe", "expert", None),
        P("pipe", "expert", None),
        P("pipe", None),
        P("pipe", None, None),
        P("pipe", "expert", None, None),
        P("pipe", "expert", None, None),
    )
    return jax.shard_map(
        per_device,
        mesh=mesh,
        in_specs=placed,
        out_specs=(P("pipe", "expert", None), P("pipe", "expert", None)),
        check_vma=False,
    )
```

```python
import jax
import jax.numpy as jnp
from jax import lax
from jax.experimental import pallas as pl
from jax.sharding import PartitionSpec as P

CAP = 32

def dispatch_kernel(x_ref, gain_ref, ids_ref, send_ref, normed_ref):
    tokens = x_ref.shape[0]
    rows = send_ref.shape[0]
    xf = x_ref[...].astype(jnp.float32)
    ms = jnp.mean(xf * xf, axis=-1, keepdims=True)
    normed = (xf * lax.rsqrt(ms + 1e-06) * gain_ref[...]).astype(jnp.bfloat16)
    normed_ref[...] = normed
    row = lax.broadcasted_iota(jnp.int32, (rows, tokens), 0)
    owner = row // CAP
    member = ids_ref[0] == owner
    for k in range(1, ids_ref.shape[0]):
        member = member | (ids_ref[k] == owner)
    member = member.astype(jnp.bfloat16)
    later = (lax.broadcasted_iota(jnp.int32, (tokens, tokens), 0)
             < lax.broadcasted_iota(jnp.int32, (tokens, tokens), 1)).astype(jnp.bfloat16)
    slot = jnp.dot(member, later, preferred_element_type=jnp.float32)
    offset = (row % CAP).astype(jnp.float32)
    place = jnp.where(slot == offset, member, jnp.zeros_like(member))
    send_ref[...] = jnp.dot(place, normed, preferred_element_type=jnp.float32).astype(jnp.bfloat16)


def dispatch(x, gain, ids, experts):
    tokens, width = x.shape
    rows = experts * CAP
    return pl.pallas_call(
        dispatch_kernel,
        out_shape=(jax.ShapeDtypeStruct((rows, width), jnp.bfloat16),
                   jax.ShapeDtypeStruct((tokens, width), jnp.bfloat16)),
    )(x, gain.reshape(1, width), jnp.transpose(ids, (2, 0, 1)))


def shifted(block, axis, distance):
    devices = range(lax.axis_size(axis))
    route = [((i - distance) % len(devices), i) for i in devices]
    return lax.ppermute(block, axis, route)


def layer_route(x, ids_block, gain, table):
    ids = ids_block[0]
    tokens_here = x.shape[0]
    experts = table.shape[1]
    choose = ids.shape[1]
    send, normed = dispatch(x, gain, ids_block, experts)
    logits = jnp.dot(normed, table, preferred_element_type=jnp.float32)
    chosen = jnp.take_along_axis(logits, ids, axis=1)
    score = jax.nn.sigmoid(chosen)
    gates = score / jnp.sum(score, axis=-1, keepdims=True)
    onehot = (ids[:, :, None] == jnp.arange(experts, dtype=jnp.int32)[None, None, :]).astype(
        jnp.int32
    )
    flat = onehot.reshape(tokens_here * choose, experts)
    before = jnp.cumsum(flat, axis=0) - flat
    slot = jnp.sum(before * flat, axis=-1).reshape(tokens_here, choose)
    target = ids * CAP + slot
    rows = jnp.arange(experts * CAP, dtype=jnp.int32)
    hit = target[:, :, None] == rows[None, None, :]
    weight = jnp.sum(jnp.where(hit, gates[:, :, None], 0.0), axis=1)
    weight_hi = weight.astype(jnp.bfloat16)
    weight_lo = (weight - weight_hi.astype(jnp.float32)).astype(jnp.bfloat16)
    return (send, weight_hi, weight_lo)


def apply_experts(rows, up_w, down_w):
    up_h = jnp.dot(rows, up_w, preferred_element_type=jnp.float32)
    hidden = jax.nn.silu(up_h).astype(jnp.bfloat16)
    return jnp.dot(hidden, down_w, preferred_element_type=jnp.float32).astype(jnp.bfloat16)


def finish(x, weight_hi, weight_lo, returned):
    tokens_here = weight_hi.shape[0]
    both = jnp.dot(
        jnp.concatenate([weight_hi, weight_lo], axis=0), returned,
        preferred_element_type=jnp.float32,
    )
    combined = both[:tokens_here] + both[tokens_here:]
    return (x.astype(jnp.float32) + 2.5 * combined).astype(jnp.bfloat16)


def exchange(block):
    return lax.all_to_all(block, "expert", split_axis=0, concat_axis=0, tiled=True)


def per_device(up_in, down_in, up_ids, down_ids, norm_gain, router, w_up, w_down):
    gain = norm_gain[0]
    table = router[0]
    up_w = w_up[0, 0]
    down_w = w_down[0, 0]
    send_up, hi_up, lo_up = layer_route(up_in[0], up_ids, gain, table)
    send_down, hi_down, lo_down = layer_route(down_in[0], down_ids, gain, table)
    rows_up = exchange(send_up)
    rows_down = exchange(send_down)
    back_up = exchange(apply_experts(rows_up, up_w, down_w))
    back_down = exchange(apply_experts(rows_down, up_w, down_w))
    layer_up = finish(up_in[0], hi_up, lo_up, back_up)
    up_out = shifted(layer_up[None], "pipe", 1)
    layer_down = finish(down_in[0], hi_down, lo_down, back_down)
    down_out = shifted(layer_down[None], "pipe", -1)
    return (up_out, down_out)


def solution(mesh):
    placed = (
        P("pipe", "expert", None),
        P("pipe", "expert", None),
        P("pipe", "expert", None),
        P("pipe", "expert", None),
        P("pipe", None),
        P("pipe", None, None),
        P("pipe", "expert", None, None),
        P("pipe", "expert", None, None),
    )
    return jax.shard_map(
        per_device,
        mesh=mesh,
        in_specs=placed,
        out_specs=(P("pipe", "expert", None), P("pipe", "expert", None)),
        check_vma=False,
    )
```
